128 devices in a mesh: seq: 16 (over z, x), exp: 8 (over y, core).
Axes of the slice: x: 4, y: 4, z: 4, core: 2. Of those that a mesh axis runs over, the one named last changes fastest.
Arguments:
- residual_in: bfloat16 [8, 4096, 2048], P('exp', 'seq'), may hold values from -6 to 6
- query_matrix: bfloat16 [8, 4096, 2048], P('exp', 'seq'), may hold values from -6 to 6
- key_vectors: bfloat16 [8, 4096, 2048], P('exp', 'seq'), may hold values from -6 to 6
- value_vectors: bfloat16 [8, 4096, 2048], P('exp', 'seq'), may hold values from -6 to 6
- head_gain: float32 [2048], replicated, may hold values from 0.5 to 1.5
- norm_gain: float32 [2048], replicated, may hold values from 0.5 to 1.5
- expert_ids: int32 [8, 4096, 4], P('exp', 'seq'), may hold values from 0 to 7, all different within a row; in each aligned block of 256 rows (0 to 255, 256 to 511, ..., all dimensions but the last counted through in order) at most 192 rows name the same one
- gate_probs: float32 [8, 4096, 4], P('exp', 'seq'), may hold values from 0.25 to 1
- w_gate: bfloat16 [8, 2048, 1408], P('exp'), may hold values from -0.125 to 0.125
- w_up: bfloat16 [8, 2048, 1408], P('exp'), may hold values from -0.125 to 0.125
- w_down: bfloat16 [8, 1408, 2048], P('exp'), may hold values from -0.15625 to 0.15625
Outputs:
- layer_out: bfloat16 [8, 4096, 2048], P('exp', 'seq')
The draws below stay inside these ranges and needn't reach their ends.
Inputs may be any that keep to these rules, and one draw needn't show every extreme that they name: `expert_ids`: the 4 experts of one position differ; among the 256 positions of one device, no expert is named by more than 192 routes.
All inputs are finite; a program needn't handle non-finite values.
Results may differ from the reference program's by a relative error of at most 0.013.
Values may be sent and summed in bfloat16 or wider, within the bound.
No kernel may reach another device: no remote copies, remote signals or barrier semaphores. Data moves between devices by JAX's collectives and lax.ppermute only.
A program may use at most 128 MiB of HBM per device.

```python
import math
import jax
import jax.numpy as jnp
import numpy as np
from jax import lax

D = 2048
HEADS = 16
HD = 128
FF = 1408
TOP = 4
EXPERTS = 8
TOK_DEV = 256
LEN = 4096
SEQS = 8
CAP = 192


def steps_of(key, extent, shards, least, top_value):
    def one(dim, blocks):
        heights = jax.random.uniform(jax.random.fold_in(jax.random.fold_in(key, 6), dim), (blocks,), jnp.float32, least / len(shards), top_value / len(shards))
        return jnp.repeat(jnp.exp(heights), extent[dim] // blocks).reshape((-1,) + (1,) * (len(extent) - dim - 1))

    loudness = one(*shards[0])
    for cut in shards[1:]:
        loudness = loudness * one(*cut)
    return loudness


def routed_block(key, own, number, rows, amount, top, most, skew):
    ranking = jax.random.permutation(key, amount)
    packed, common = shares(amount, rows * top, most, skew, True), shares(amount, rows * top, most, skew, False)
    places = jnp.arange(amount)

    def named(sizes, offset_by):
        used = int((sizes > 0).sum())
        fixed = max(1, used // 4)
        shifted = fixed + (places - fixed + offset_by * (used - fixed)) % max(1, amount - fixed)
        return jnp.zeros((amount,), jnp.int32).at[ranking[jnp.where(places < fixed, places, shifted)]].set(jnp.asarray(sizes, jnp.int32))

    sizes = jnp.where(number % 4 == 0, named(packed, number // 4), named(common, number - number // 4 - 1))
    mixed = jax.random.permutation(jax.random.fold_in(own, 3), amount)
    source_of, taker = mixed[0:amount // 2 * 2:2], mixed[1:amount // 2 * 2:2]
    margin = jnp.minimum(sizes[source_of] - 1, most - sizes[taker]) // 2
    margin = jnp.where((source_of == ranking[0]) | (taker == ranking[0]) | (sizes[taker] == 0), 0, jnp.maximum(margin, 0))
    shifted = jax.random.randint(jax.random.fold_in(own, 4), (amount // 2,), 0, 1 << 20) % (margin + 1)
    sizes = sizes.at[source_of].add(-shifted).at[taker].add(shifted)
    members = jnp.searchsorted(jnp.cumsum(sizes), jnp.arange(rows * top), side="right").astype(jnp.int32)
    listing = members.reshape(top, rows).T
    listing = listing[jax.random.permutation(jax.random.fold_in(own, 1), rows)]
    offset_by = jax.random.randint(jax.random.fold_in(own, 2), (rows, 1), 0, top)
    return jnp.take_along_axis(listing, (jnp.arange(top)[None, :] + offset_by) % top, axis=1)


def shares(number_of, total, most, skew, full):
    weights = [(1 << 20) // math.isqrt(standing ** skew) + 1 for standing in range(1, number_of + 1)]
    largest = most if full else min(most, max(-(-total // number_of), total * weights[0] // sum(weights)))
    least = 1 if total - largest >= number_of - 1 else 0
    holding, surplus = [largest] + [least] * (number_of - 1), total - largest - least * (number_of - 1)
    while surplus > 0:
        free = [i for i in range(1, number_of) if holding[i] < largest] or [i for i in range(1, number_of) if holding[i] < most]
        whole, remaining = sum([weights[i] for i in free]), surplus
        for i in free:
            addition = min(most - holding[i], max(1, remaining * weights[i] // whole), surplus)
            holding[i] = holding[i] + addition
            surplus = surplus - addition
    return np.array(holding)


def scatter_about(rng, extent, width, bound, cuts=(), held_as=jnp.bfloat16):
    array = width * jax.random.normal(rng, extent, jnp.float32)
    if cuts:
        array = array * steps_of(rng, extent, cuts, -0.22, 0.18)
    return jnp.clip(array, -bound, bound).astype(held_as)


def setup_inputs(seed: int = 0) -> dict:
    splits = jax.random.split(jax.random.key(seed), 12)
    residual_in = scatter_about(splits[0], (SEQS, LEN, D), 1.0, 6.0, ((0, 8), (1, 16)))
    query_matrix = scatter_about(splits[1], (SEQS, LEN, D), 1.0, 6.0, ((0, 8), (1, 16)))
    key_vectors = scatter_about(splits[2], (SEQS, LEN, D), 1.0, 6.0, ((0, 8), (1, 16)))
    value_vectors = scatter_about(splits[3], (SEQS, LEN, D), 1.0, 6.0, ((0, 8), (1, 16)))
    head_gain = jnp.clip(1.0 + 0.1 * jax.random.normal(splits[4], (D,), jnp.float32), 0.5, 1.5)
    norm_gain = jnp.clip(1.0 + 0.1 * jax.random.normal(splits[5], (D,), jnp.float32), 0.5, 1.5)
    expert_ids_keys = jax.random.split(jax.random.fold_in(splits[6], 1), SEQS * LEN // TOK_DEV)
    expert_ids_turns = jax.random.permutation(jax.random.fold_in(splits[6], 3), SEQS * LEN // TOK_DEV)
    expert_ids = jax.vmap(lambda own, number: routed_block(jax.random.fold_in(splits[6], 2), own, number, TOK_DEV, EXPERTS, TOP, CAP, 2))(expert_ids_keys, expert_ids_turns).reshape((SEQS, LEN, TOP))
    gate_probs = jnp.clip(0.25 + 0.75 * jax.random.uniform(splits[7], (SEQS, LEN, TOP), jnp.float32) ** steps_of(splits[7], (SEQS, LEN, TOP), ((0, 8), (1, 16)), -0.2, 0.2), 0.25, 1.0)
    w_gate = scatter_about(splits[8], (EXPERTS, D, FF), D ** -0.5, 0.125, ((0, 8),))
    w_up = scatter_about(splits[9], (EXPERTS, D, FF), D ** -0.5, 0.125, ((0, 8),))
    w_down = scatter_about(splits[10], (EXPERTS, FF, D), FF ** -0.5, 0.15625, ((0, 8),))
    return {"residual_in": residual_in, "query_matrix": query_matrix, "key_vectors": key_vectors, "value_vectors": value_vectors, "head_gain": head_gain, "norm_gain": norm_gain, "expert_ids": expert_ids, "gate_probs": gate_probs, "w_gate": w_gate, "w_up": w_up, "w_down": w_down}


def reference(residual_in, query_matrix, key_vectors, value_vectors, head_gain, norm_gain, expert_ids, gate_probs, w_gate, w_up, w_down):
    nblocks = LEN // TOK_DEV

    def split_heads(arr):
        return arr.astype(jnp.float32).reshape(SEQS, nblocks, TOK_DEV, HEADS, HD)
    queries = split_heads(query_matrix)
    key_rows = split_heads(key_vectors)
    value_rows = split_heads(value_vectors)
    states = jnp.einsum('sbthd,sbthe->sbhde', key_rows, value_rows)
    running = jnp.cumsum(states, axis=1)
    prefix = jnp.concatenate([jnp.zeros_like(states[:, :1]), running[:, :-1]], axis=1)
    prefix = lax.optimization_barrier(prefix.astype(jnp.bfloat16)).astype(jnp.float32)
    causal = jnp.tril(jnp.ones((TOK_DEV, TOK_DEV), dtype=bool))

    def per_sequence(item_entries):
        query_row_block, key_row_block, value_row_block, partial_state = item_entries
        scores = jnp.einsum('bthd,buhd->bhtu', query_row_block, key_row_block)
        weights = jnp.where(causal[None, None], scores, 0.0).astype(jnp.bfloat16)
        weights = lax.optimization_barrier(weights).astype(jnp.float32)
        inner = jnp.einsum('bhtu,buhd->bthd', weights, value_row_block)
        outer_product = jnp.einsum('urpw,upwa->urpa', query_row_block, partial_state)
        return inner + outer_product
    mixed = lax.map(per_sequence, (queries, key_rows, value_rows, prefix))
    mean_square = lax.optimization_barrier(jnp.mean(mixed * mixed, axis=-1, keepdims=True))
    attn = (mixed * lax.rsqrt(mean_square + 1e-06)).reshape(SEQS, LEN, D) * head_gain
    resid_sum = (residual_in.astype(jnp.float32) + attn).astype(jnp.bfloat16)
    resid_float = resid_sum.astype(jnp.float32)
    row_square = lax.optimization_barrier(jnp.mean(resid_float * resid_float, axis=-1, keepdims=True))
    normed = (resid_float * lax.rsqrt(row_square + 1e-06) * norm_gain).astype(jnp.bfloat16)
    rows = SEQS * LEN
    blocks = rows // TOK_DEV
    route_ids = expert_ids.reshape(blocks, TOK_DEV * TOP).astype(jnp.int32)
    expert_indicator = (route_ids[:, :, None] == jnp.arange(EXPERTS, dtype=jnp.int32)[None, None, :]).astype(jnp.int32)
    slots = lax.optimization_barrier(jnp.sum((jnp.cumsum(expert_indicator, axis=1) - expert_indicator) * expert_indicator, axis=2)).astype(jnp.int32)
    position = (jnp.arange(blocks, dtype=jnp.int32)[:, None] * CAP + slots).reshape(-1)
    token_of = (jnp.arange(blocks, dtype=jnp.int32)[:, None] * TOK_DEV + jnp.arange(TOK_DEV * TOP, dtype=jnp.int32)[None, :] // TOP).reshape(-1)
    flat_ids = route_ids.reshape(-1)
    flat_gates = gate_probs.reshape(-1).astype(jnp.float32)
    padded = jnp.concatenate([normed.reshape(rows, D), jnp.zeros((1, D), jnp.bfloat16)], axis=0)

    def one_expert(total, item_entries):
        expert, gate_mat, up_mat, down_mat = item_entries
        target = jnp.where(flat_ids == expert, position, blocks * CAP).astype(jnp.int32)
        index = jnp.full((blocks * CAP,), rows, jnp.int32).at[target].set(token_of, mode='drop')
        weight = jnp.zeros((blocks * CAP,), jnp.float32).at[target].set(flat_gates, mode='drop')
        chosen = padded[index]
        gate_part = jnp.dot(chosen, gate_mat, preferred_element_type=jnp.float32)
        up_part = jnp.dot(chosen, up_mat, preferred_element_type=jnp.float32)
        hidden = (jax.nn.silu(gate_part) * up_part).astype(jnp.bfloat16)
        result = jnp.dot(hidden, down_mat, preferred_element_type=jnp.float32).astype(jnp.bfloat16)
        total = total.at[index].add(result.astype(jnp.float32) * weight[:, None], mode='drop')
        return (total, None)
    total, _ = lax.scan(one_expert, jnp.zeros((rows, D), jnp.float32), (jnp.arange(EXPERTS, dtype=jnp.int32), w_gate, w_up, w_down))
    return (resid_float + total.reshape(SEQS, LEN, D)).astype(jnp.bfloat16)
```

```python
import jax
import jax.numpy as jnp
from jax import lax
from jax.sharding import PartitionSpec as P

D = 2048
HEADS = 16
HD = 128
TOP = 4
EXPERTS = 8


def block_prefix(state):
    blocks = lax.axis_size("seq")
    pieces = state.reshape(blocks, -1)
    gathered = lax.all_to_all(pieces, "seq", split_axis=0, concat_axis=0, tiled=True)
    running = jnp.zeros_like(gathered[0])
    sums = []
    for j in range(blocks):
        sums.append(running)
        running = running + gathered[j]
    prefixes = jnp.stack(sums).astype(jnp.bfloat16)
    mine = lax.all_to_all(prefixes, "seq", split_axis=0, concat_axis=0, tiled=True)
    return mine.reshape(state.shape)


def on_device(
    residual_in,
    query_matrix,
    key_vectors,
    value_vectors,
    head_gain,
    norm_gain,
    expert_ids,
    gate_probs,
    w_gate,
    w_up,
    w_down,
):
    positions = residual_in.shape[1]
    queries = query_matrix[0].reshape(positions, HEADS, HD)
    key_rows = key_vectors[0].reshape(positions, HEADS, HD)
    value_rows = value_vectors[0].reshape(positions, HEADS, HD)
    state = jnp.einsum("thd,the->hde", key_rows, value_rows, preferred_element_type=jnp.float32)
    prefix = block_prefix(state)
    causal = jnp.tril(jnp.ones((positions, positions), dtype=bool))
    scores = jnp.einsum("thd,uhd->htu", queries, key_rows, preferred_element_type=jnp.float32)
    weights = jnp.where(causal[None], scores, 0.0).astype(jnp.bfloat16)
    inner = jnp.einsum("htu,uhd->thd", weights, value_rows, preferred_element_type=jnp.float32)
    outer_product = jnp.einsum(
        "thd,hde->the", queries, prefix, preferred_element_type=jnp.float32
    )
    mixed = inner + outer_product
    mean_square = jnp.mean(mixed * mixed, axis=-1, keepdims=True)
    attn = (mixed * lax.rsqrt(mean_square + 1e-06)).reshape(positions, D) * head_gain
    resid_float = (
        (residual_in[0].astype(jnp.float32) + attn).astype(jnp.bfloat16).astype(jnp.float32)
    )
    row_square = jnp.mean(resid_float * resid_float, axis=-1, keepdims=True)
    normed = (resid_float * lax.rsqrt(row_square + 1e-06) * norm_gain).astype(jnp.bfloat16)

    route_ids = expert_ids[0]
    route_gates = gate_probs[0]
    experts = jnp.arange(EXPERTS, dtype=jnp.int32)
    table = jnp.sum(
        jnp.where(route_ids[:, :, None] == experts[None, None, :], route_gates[:, :, None], 0.0),
        axis=1,
    )
    local_count = w_gate.shape[0]
    rows = lax.all_gather(normed, "exp", axis=0, tiled=True)
    all_table = lax.all_gather(table, "exp", axis=0, tiled=True)
    first = lax.axis_index("exp") * local_count
    local_weights = lax.dynamic_slice_in_dim(all_table, first, local_count, axis=1)
    gate_part = jnp.einsum("nd,edf->enf", rows, w_gate, preferred_element_type=jnp.float32)
    up_part = jnp.einsum("nd,edf->enf", rows, w_up, preferred_element_type=jnp.float32)
    hidden = (jax.nn.silu(gate_part) * up_part).astype(jnp.bfloat16)
    result = jnp.einsum("enf,efd->end", hidden, w_down, preferred_element_type=jnp.float32)
    result = result.astype(jnp.bfloat16).astype(jnp.float32)
    contrib = jnp.sum(result * local_weights.T[:, :, None], axis=0).astype(jnp.bfloat16)
    combined = lax.psum_scatter(contrib, "exp", scatter_dimension=0, tiled=True)
    return (resid_float + combined.astype(jnp.float32)).astype(jnp.bfloat16)[None]


def solution(mesh):
    in_specs = (
        P("exp", "seq", None),
        P("exp", "seq", None),
        P("exp", "seq", None),
        P("exp", "seq", None),
        P(),
        P(),
        P("exp", "seq", None),
        P("exp", "seq", None),
        P("exp", None, None),
        P("exp", None, None),
        P("exp", None, None),
    )
    out_specs = P("exp", "seq", None)
    return jax.shard_map(
        on_device, mesh=mesh, in_specs=in_specs, out_specs=out_specs, check_vma=False
    )
```

```python
import jax
import jax.numpy as jnp
from jax import lax
from jax.sharding import PartitionSpec as P

D = 2048
HEADS = 16
HD = 128
TOP = 4
EXPERTS = 8
CHUNKS = 2


def block_prefix(state):
    blocks = lax.axis_size("seq")
    pieces = state.reshape(blocks, -1)
    gathered = lax.all_to_all(pieces, "seq", split_axis=0, concat_axis=0, tiled=True)
    shifted = jnp.concatenate([jnp.zeros_like(gathered[:1]), gathered[:-1]], axis=0)
    prefixes = lax.cumsum(shifted, axis=0).astype(jnp.bfloat16)
    mine = lax.all_to_all(prefixes, "seq", split_axis=0, concat_axis=0, tiled=True)
    return mine.reshape(state.shape)


def on_device(
    residual_in,
    query_matrix,
    key_vectors,
    value_vectors,
    head_gain,
    norm_gain,
    expert_ids,
    gate_probs,
    w_gate,
    w_up,
    w_down,
):
    positions = residual_in.shape[1]
    queries = query_matrix[0].reshape(positions, HEADS, HD)
    key_rows = key_vectors[0].reshape(positions, HEADS, HD)
    value_rows = value_vectors[0].reshape(positions, HEADS, HD)
    state = jnp.einsum("thd,the->hde", key_rows, value_rows, preferred_element_type=jnp.float32)
    prefix = block_prefix(state)
    causal = jnp.tril(jnp.ones((positions, positions), dtype=bool))
    scores = jnp.einsum("thd,uhd->htu", queries, key_rows, preferred_element_type=jnp.float32)
    weights = jnp.where(causal[None], scores, 0.0).astype(jnp.bfloat16)
    inner = jnp.einsum("htu,uhd->thd", weights, value_rows, preferred_element_type=jnp.float32)
    outer_product = jnp.einsum(
        "thd,hde->the", queries, prefix, preferred_element_type=jnp.float32
    )
    mixed = inner + outer_product
    mean_square = jnp.mean(mixed * mixed, axis=-1, keepdims=True)
    attn = (mixed * lax.rsqrt(mean_square + 1e-06)).reshape(positions, D) * head_gain
    resid_float = (
        (residual_in[0].astype(jnp.float32) + attn).astype(jnp.bfloat16).astype(jnp.float32)
    )
    row_square = jnp.mean(resid_float * resid_float, axis=-1, keepdims=True)
    normed = (resid_float * lax.rsqrt(row_square + 1e-06) * norm_gain).astype(jnp.bfloat16)

    route_ids = expert_ids[0]
    route_gates = gate_probs[0]
    experts = jnp.arange(EXPERTS, dtype=jnp.int32)
    table = jnp.sum(
        jnp.where(route_ids[:, :, None] == experts[None, None, :], route_gates[:, :, None], 0.0),
        axis=1,
    )
    groups = lax.axis_size("exp")
    me = lax.axis_index("exp")
    slots = jnp.where((jnp.arange(groups) == me)[:, None, None], table[None], 0.0)
    all_table = lax.psum(slots, "exp")
    local_count = w_gate.shape[0]
    local_weights = lax.dynamic_slice_in_dim(all_table, me * local_count, local_count, axis=2)

    chunk = positions // CHUNKS
    outs = []
    for c in range(CHUNKS):
        part = normed[c * chunk:(c + 1) * chunk]
        rows = lax.all_gather(part, "exp", axis=0, tiled=True)
        weight = local_weights[:, c * chunk:(c + 1) * chunk].reshape(groups * chunk, local_count)
        gate_part = jnp.einsum("nd,edf->enf", rows, w_gate, preferred_element_type=jnp.float32)
        up_part = jnp.einsum("nd,edf->enf", rows, w_up, preferred_element_type=jnp.float32)
        hidden = (jax.nn.silu(gate_part) * up_part).astype(jnp.bfloat16)
        result = jnp.einsum("enf,efd->end", hidden, w_down, preferred_element_type=jnp.float32)
        result = result.astype(jnp.bfloat16).astype(jnp.float32)
        contrib = jnp.sum(result * weight.T[:, :, None], axis=0).astype(jnp.bfloat16)
        outs.append(lax.psum_scatter(contrib, "exp", scatter_dimension=0, tiled=True))
    combined = jnp.concatenate(outs, axis=0)
    return (resid_float + combined.astype(jnp.float32)).astype(jnp.bfloat16)[None]


def solution(mesh):
    in_specs = (
        P("exp", "seq", None),
        P("exp", "seq", None),
        P("exp", "seq", None),
        P("exp", "seq", None),
        P(),
        P(),
        P("exp", "seq", None),
        P("exp", "seq", None),
        P("exp", None, None),
        P("exp", None, None),
        P("exp", None, None),
    )
    out_specs = P("exp", "seq", None)
    return jax.shard_map(
        on_device, mesh=mesh, in_specs=in_specs, out_specs=out_specs, check_vma=False
    )
```

```python
import jax
import jax.numpy as jnp
from jax import lax
from jax.sharding import PartitionSpec as P

D = 2048
HEADS = 16
HD = 128
TOP = 4
EXPERTS = 8
CHUNKS = 2


def block_prefix(state):
    blocks = lax.axis_size("seq")
    pieces = state.reshape(blocks, -1)
    gathered = lax.all_to_all(pieces, "seq", split_axis=0, concat_axis=0, tiled=True)
    shifted = jnp.concatenate([jnp.zeros_like(gathered[:1]), gathered[:-1]], axis=0)
    prefixes = lax.cumsum(shifted, axis=0).astype(jnp.bfloat16)
    mine = lax.all_to_all(prefixes, "seq", split_axis=0, concat_axis=0, tiled=True)
    return mine.reshape(state.shape)


def on_device(
    residual_in,
    query_matrix,
    key_vectors,
    value_vectors,
    head_gain,
    norm_gain,
    expert_ids,
    gate_probs,
    w_gate,
    w_up,
    w_down,
):
    positions = residual_in.shape[1]
    queries = query_matrix[0].reshape(positions, HEADS, HD)
    key_rows = key_vectors[0].reshape(positions, HEADS, HD)
    value_rows = value_vectors[0].reshape(positions, HEADS, HD)
    state = jnp.einsum("thd,the->hde", key_rows, value_rows, preferred_element_type=jnp.float32)
    prefix = block_prefix(state)
    causal = jnp.tril(jnp.ones((positions, positions), dtype=bool))
    scores = jnp.einsum("thd,uhd->htu", queries, key_rows, preferred_element_type=jnp.float32)
    weights = jnp.where(causal[None], scores, 0.0).astype(jnp.bfloat16)
    inner = jnp.einsum("htu,uhd->thd", weights, value_rows, preferred_element_type=jnp.float32)
    outer_product = jnp.einsum(
        "thd,hde->the", queries, prefix, preferred_element_type=jnp.float32
    )
    mixed = inner + outer_product
    mean_square = jnp.mean(mixed * mixed, axis=-1, keepdims=True)
    attn = (mixed * lax.rsqrt(mean_square + 1e-06)).reshape(positions, D) * head_gain
    resid_float = (
        (residual_in[0].astype(jnp.float32) + attn).astype(jnp.bfloat16).astype(jnp.float32)
    )
    row_square = jnp.mean(resid_float * resid_float, axis=-1, keepdims=True)
    normed = (resid_float * lax.rsqrt(row_square + 1e-06) * norm_gain).astype(jnp.bfloat16)

    route_ids = expert_ids[0]
    route_gates = gate_probs[0]
    experts = jnp.arange(EXPERTS, dtype=jnp.int32)
    table = jnp.sum(
        jnp.where(route_ids[:, :, None] == experts[None, None, :], route_gates[:, :, None], 0.0),
        axis=1,
    )
    groups = lax.axis_size("exp")
    me = lax.axis_index("exp")
    local_count = w_gate.shape[0]
    high = table.astype(jnp.bfloat16)
    rest = table - high.astype(jnp.float32)
    middle = rest.astype(jnp.bfloat16)
    low = (rest - middle.astype(jnp.float32)).astype(jnp.bfloat16)
    pad = jnp.zeros((positions, 128 - 3 * EXPERTS), jnp.bfloat16)
    payload = jnp.concatenate([normed, high, middle, low, pad], axis=1)

    chunk = positions // CHUNKS
    outs = []
    for c in range(CHUNKS):
        gathered = lax.all_gather(payload[c * chunk:(c + 1) * chunk], "exp", axis=0, tiled=True)
        rows = gathered[:, :D]
        code = gathered[:, D:D + 3 * EXPERTS].astype(jnp.float32)
        code = lax.dynamic_slice_in_dim(code.reshape(-1, 3, EXPERTS), me * local_count, local_count, axis=2)
        weight = code[:, 0] + code[:, 1] + code[:, 2]
        gate_part = jnp.einsum("nd,edf->enf", rows, w_gate, preferred_element_type=jnp.float32)
        up_part = jnp.einsum("nd,edf->enf", rows, w_up, preferred_element_type=jnp.float32)
        hidden = (jax.nn.silu(gate_part) * up_part).astype(jnp.bfloat16)
        result = jnp.einsum("enf,efd->end", hidden, w_down, preferred_element_type=jnp.float32)
        result = result.astype(jnp.bfloat16).astype(jnp.float32)
        contrib = jnp.sum(result * weight.T[:, :, None], axis=0).astype(jnp.bfloat16)
        outs.append(lax.psum_scatter(contrib, "exp", scatter_dimension=0, tiled=True))
    combined = jnp.concatenate(outs, axis=0)
    return (resid_float + combined.astype(jnp.float32)).astype(jnp.bfloat16)[None]


def solution(mesh):
    in_specs = (
        P("exp", "seq", None),
        P("exp", "seq", None),
        P("exp", "seq", None),
        P("exp", "seq", None),
        P(),
        P(),
        P("exp", "seq", None),
        P("exp", "seq", None),
        P("exp", None, None),
        P("exp", None, None),
        P("exp", None, None),
    )
    out_specs = P("exp", "seq", None)
    return jax.shard_map(
        on_device, mesh=mesh, in_specs=in_specs, out_specs=out_specs, check_vma=False
    )
```

```python
import jax
import jax.numpy as jnp
from jax import lax
from jax.sharding import PartitionSpec as P

D = 2048
HEADS = 16
HD = 128
TOP = 4
EXPERTS = 8
CHUNKS = 1


def block_prefix(state):
    blocks = lax.axis_size("seq")
    pieces = state if blocks == state.shape[0] else state.reshape(blocks, -1)
    gathered = lax.all_to_all(pieces, "seq", split_axis=0, concat_axis=0, tiled=True)
    shifted = jnp.concatenate([jnp.zeros_like(gathered[:1]), gathered[:-1]], axis=0)
    prefixes = lax.cumsum(shifted, axis=0).astype(jnp.bfloat16)
    mine = lax.all_to_all(prefixes, "seq", split_axis=0, concat_axis=0, tiled=True)
    return mine.reshape(state.shape)


def on_device(
    residual_in,
    query_matrix,
    key_vectors,
    value_vectors,
    head_gain,
    norm_gain,
    expert_ids,
    gate_probs,
    w_gate,
    w_up,
    w_down,
):
    positions = residual_in.shape[1]
    queries = query_matrix[0].reshape(positions, HEADS, HD)
    key_rows = key_vectors[0].reshape(positions, HEADS, HD)
    value_rows = value_vectors[0].reshape(positions, HEADS, HD)
    state = jnp.einsum("thd,the->hde", key_rows, value_rows, preferred_element_type=jnp.float32)
    prefix = block_prefix(state)
    causal = jnp.tril(jnp.ones((positions, positions), dtype=bool))
    scores = jnp.einsum("thd,uhd->htu", queries, key_rows, preferred_element_type=jnp.float32)
    weights = jnp.where(causal[None], scores, 0.0).astype(jnp.bfloat16)
    inner = jnp.einsum("htu,uhd->thd", weights, value_rows, preferred_element_type=jnp.float32)
    outer_product = jnp.einsum(
        "thd,hde->the", queries, prefix, preferred_element_type=jnp.float32
    )
    mixed = inner + outer_product
    mean_square = jnp.mean(mixed * mixed, axis=-1, keepdims=True)
    attn = (mixed * lax.rsqrt(mean_square + 1e-06)).reshape(positions, D) * head_gain
    resid_float = (
        (residual_in[0].astype(jnp.float32) + attn).astype(jnp.bfloat16).astype(jnp.float32)
    )
    row_square = jnp.mean(resid_float * resid_float, axis=-1, keepdims=True)
    normed = (resid_float * lax.rsqrt(row_square + 1e-06) * norm_gain).astype(jnp.bfloat16)

    route_ids = expert_ids[0]
    route_gates = gate_probs[0]
    experts = jnp.arange(EXPERTS, dtype=jnp.int32)
    table = jnp.sum(
        jnp.where(route_ids[:, :, None] == experts[None, None, :], route_gates[:, :, None], 0.0),
        axis=1,
    )
    groups = lax.axis_size("exp")
    me = lax.axis_index("exp")
    local_count = w_gate.shape[0]
    high = table.astype(jnp.bfloat16)
    rest = table - high.astype(jnp.float32)
    middle = rest.astype(jnp.bfloat16)
    low = (rest - middle.astype(jnp.float32)).astype(jnp.bfloat16)
    pad = jnp.zeros((positions, 128 - 3 * EXPERTS), jnp.bfloat16)
    payload = jnp.concatenate([normed, high, middle, low, pad], axis=1)

    chunk = positions // CHUNKS
    outs = []
    for c in range(CHUNKS):
        gathered = lax.all_gather(payload[c * chunk:(c + 1) * chunk], "exp", axis=0, tiled=True)
        rows = gathered[:, :D]
        code = gathered[:, D:D + 3 * EXPERTS].astype(jnp.float32)
        code = lax.dynamic_slice_in_dim(code.reshape(-1, 3, EXPERTS), me * local_count, local_count, axis=2)
        weight = code[:, 0] + code[:, 1] + code[:, 2]
        gate_part = jnp.einsum("nd,edf->enf", rows, w_gate, preferred_element_type=jnp.float32)
        up_part = jnp.einsum("nd,edf->enf", rows, w_up, preferred_element_type=jnp.float32)
        hidden = (jax.nn.silu(gate_part) * up_part).astype(jnp.bfloat16)
        result = jnp.einsum("enf,efd->end", hidden, w_down, preferred_element_type=jnp.float32)
        result = result.astype(jnp.bfloat16).astype(jnp.float32)
        contrib = jnp.sum(result * weight.T[:, :, None], axis=0).astype(jnp.bfloat16)
        outs.append(lax.psum_scatter(contrib, "exp", scatter_dimension=0, tiled=True))
    combined = jnp.concatenate(outs, axis=0)
    return (resid_float + combined.astype(jnp.float32)).astype(jnp.bfloat16)[None]


def solution(mesh):
    in_specs = (
        P("exp", "seq", None),
        P("exp", "seq", None),
        P("exp", "seq", None),
        P("exp", "seq", None),
        P(),
        P(),
        P("exp", "seq", None),
        P("exp", "seq", None),
        P("exp", None, None),
        P("exp", None, None),
        P("exp", None, None),
    )
    out_specs = P("exp", "seq", None)
    return jax.shard_map(
        on_device, mesh=mesh, in_specs=in_specs, out_specs=out_specs, check_vma=False
    )
```

```python
import jax
import jax.numpy as jnp
from jax import lax
from jax.experimental.layout import Layout, with_layout_constraint
from jax.sharding import PartitionSpec as P


D = 2048
HEADS = 16
HD = 128
EXPERTS = 8
CHUNKS = 2


def block_prefix(state):
    blocks = lax.axis_size("seq")
    pieces = state if blocks == state.shape[0] else state.reshape(blocks, -1)
    gathered = lax.all_to_all(pieces, "seq", split_axis=0, concat_axis=0, tiled=True)
    shifted = jnp.concatenate([jnp.zeros_like(gathered[:1]), gathered[:-1]], axis=0)
    prefixes = lax.cumsum(shifted, axis=0).astype(jnp.bfloat16)
    mine = lax.all_to_all(prefixes, "seq", split_axis=0, concat_axis=0, tiled=True)
    return mine.reshape(state.shape)


def on_device(
    residual_in,
    query_matrix,
    key_vectors,
    value_vectors,
    head_gain,
    norm_gain,
    expert_ids,
    gate_probs,
    w_gate,
    w_up,
    w_down,
):
    positions = residual_in.shape[1]
    queries = query_matrix[0].reshape(positions, HEADS, HD)
    key_rows = key_vectors[0].reshape(positions, HEADS, HD)
    value_rows = value_vectors[0].reshape(positions, HEADS, HD)
    state = jnp.einsum("thd,the->hed", key_rows, value_rows, preferred_element_type=jnp.float32)
    prefix = block_prefix(state)
    causal = jnp.tril(jnp.ones((positions, positions), dtype=bool))
    scores = jnp.einsum("thd,uhd->htu", queries, key_rows, preferred_element_type=jnp.float32)
    weights = jnp.where(causal[None], scores, 0.0).astype(jnp.bfloat16)
    inner = jnp.einsum("htu,uhd->thd", weights, value_rows, preferred_element_type=jnp.float32)
    outer_product = jnp.einsum(
        "thd,hed->the", queries, prefix, preferred_element_type=jnp.float32
    )
    mixed = inner + outer_product
    mean_square = jnp.mean(mixed * mixed, axis=-1, keepdims=True)
    attn = (mixed * lax.rsqrt(mean_square + 1e-06)).reshape(positions, D) * head_gain
    attn = with_layout_constraint(attn, Layout(major_to_minor=(0, 1)))
    resid_float = (
        (residual_in[0].astype(jnp.float32) + attn).astype(jnp.bfloat16).astype(jnp.float32)
    )
    row_square = jnp.mean(resid_float * resid_float, axis=-1, keepdims=True)
    normed = (resid_float * lax.rsqrt(row_square + 1e-06) * norm_gain).astype(jnp.bfloat16)

    route_ids = expert_ids[0]
    route_gates = gate_probs[0]
    experts = jnp.arange(EXPERTS, dtype=jnp.int32)
    table = jnp.sum(
        jnp.where(route_ids[:, :, None] == experts[None, None, :], route_gates[:, :, None], 0.0),
        axis=1,
    )
    me = lax.axis_index("exp")
    local_count = w_gate.shape[0]
    high = table.astype(jnp.bfloat16)
    rest = table - high.astype(jnp.float32)
    middle = rest.astype(jnp.bfloat16)
    low = (rest - middle.astype(jnp.float32)).astype(jnp.bfloat16)
    pad = jnp.zeros((positions, 128 - 3 * EXPERTS), jnp.bfloat16)
    payload = jnp.concatenate([normed, high, middle, low, pad], axis=1)

    columns = jnp.arange(3 * EXPERTS, dtype=jnp.int32) % EXPERTS
    select = (columns[:, None] == me * local_count + jnp.arange(local_count)[None, :]).astype(jnp.bfloat16)
    chunk = positions // CHUNKS
    outs = []
    for c in range(CHUNKS):
        gathered = lax.all_gather(payload[c * chunk:(c + 1) * chunk], "exp", axis=0, tiled=True)
        rows = gathered[:, :D]
        code = gathered[:, D:D + 3 * EXPERTS]
        weight = jnp.dot(code, select, preferred_element_type=jnp.float32)
        gate_part = jnp.einsum("nd,edf->enf", rows, w_gate, preferred_element_type=jnp.float32)
        up_part = jnp.einsum("nd,edf->enf", rows, w_up, preferred_element_type=jnp.float32)
        hidden = (jax.nn.silu(gate_part) * up_part).astype(jnp.bfloat16)
        result = jnp.einsum("enf,efd->end", hidden, w_down, preferred_element_type=jnp.float32)
        result = result.astype(jnp.bfloat16).astype(jnp.float32)
        contrib = jnp.sum(result * weight.T[:, :, None], axis=0).astype(jnp.bfloat16)
        outs.append(lax.psum_scatter(contrib, "exp", scatter_dimension=0, tiled=True))
    combined = jnp.concatenate(outs, axis=0)
    return (resid_float + combined.astype(jnp.float32)).astype(jnp.bfloat16)[None]


def solution(mesh):
    in_specs = (
        P("exp", "seq", None),
        P("exp", "seq", None),
        P("exp", "seq", None),
        P("exp", "seq", None),
        P(),
        P(),
        P("exp", "seq", None),
        P("exp", "seq", None),
        P("exp", None, None),
        P("exp", None, None),
        P("exp", None, None),
    )
    out_specs = P("exp", "seq", None)

    return jax.shard_map(on_device, mesh=mesh, in_specs=in_specs, out_specs=out_specs, check_vma=False)
```

```python
import jax
import jax.numpy as jnp
from jax import lax
from jax.experimental.layout import Layout, with_layout_constraint
from jax.sharding import PartitionSpec as P


D = 2048
HEADS = 16
HD = 128
EXPERTS = 8
CHUNKS = 2


def block_prefix(state):
    blocks = lax.axis_size("seq")
    pieces = state if blocks == state.shape[0] else state.reshape(blocks, -1)
    gathered = lax.all_to_all(pieces, "seq", split_axis=0, concat_axis=0, tiled=True)
    shifted = jnp.concatenate([jnp.zeros_like(gathered[:1]), gathered[:-1]], axis=0)
    prefixes = lax.cumsum(shifted, axis=0).astype(jnp.bfloat16)
    mine = lax.all_to_all(prefixes, "seq", split_axis=0, concat_axis=0, tiled=True)
    return mine.reshape(state.shape)


def on_device(
    residual_in,
    query_matrix,
    key_vectors,
    value_vectors,
    head_gain,
    norm_gain,
    expert_ids,
    gate_probs,
    w_gate,
    w_up,
    w_down,
):
    positions = residual_in.shape[1]
    queries = query_matrix[0].reshape(positions, HEADS, HD)
    key_rows = key_vectors[0].reshape(positions, HEADS, HD)
    value_rows = value_vectors[0].reshape(positions, HEADS, HD)
    state = jnp.einsum("thd,the->hed", key_rows, value_rows, preferred_element_type=jnp.float32)
    prefix = block_prefix(state)
    causal = jnp.tril(jnp.ones((positions, positions), dtype=bool))
    scores = jnp.einsum("thd,uhd->htu", queries, key_rows, preferred_element_type=jnp.float32)
    weights = jnp.where(causal[None], scores, 0.0).astype(jnp.bfloat16)
    inner = jnp.einsum("htu,uhd->thd", weights, value_rows, preferred_element_type=jnp.float32)
    outer_product = jnp.einsum(
        "thd,hed->the", queries, prefix, preferred_element_type=jnp.float32
    )
    mixed = inner + outer_product
    mean_square = jnp.mean(mixed * mixed, axis=-1, keepdims=True)
    attn = (mixed * lax.rsqrt(mean_square + 1e-06)).reshape(positions, D) * head_gain
    attn = with_layout_constraint(attn, Layout(major_to_minor=(0, 1)))
    resid_float = (
        (residual_in[0].astype(jnp.float32) + attn).astype(jnp.bfloat16).astype(jnp.float32)
    )
    row_square = jnp.mean(resid_float * resid_float, axis=-1, keepdims=True)
    normed = (resid_float * lax.rsqrt(row_square + 1e-06) * norm_gain).astype(jnp.bfloat16)

    route_ids = expert_ids[0]
    route_gates = gate_probs[0]
    experts = jnp.arange(EXPERTS, dtype=jnp.int32)
    table = jnp.sum(
        jnp.where(route_ids[:, :, None] == experts[None, None, :], route_gates[:, :, None], 0.0),
        axis=1,
    )
    cores = lax.axis_size("core")
    me = lax.axis_index("y") * cores + lax.axis_index("core")
    local_count = w_gate.shape[0]
    high = table.astype(jnp.bfloat16)
    rest = table - high.astype(jnp.float32)
    middle = rest.astype(jnp.bfloat16)
    low = (rest - middle.astype(jnp.float32)).astype(jnp.bfloat16)
    pad = jnp.zeros((positions, 128 - 3 * EXPERTS), jnp.bfloat16)
    payload = jnp.concatenate([normed, high, middle, low, pad], axis=1)
    columns = jnp.arange(3 * EXPERTS, dtype=jnp.int32) % EXPERTS
    select = (columns[:, None] == me * local_count + jnp.arange(local_count)[None, :]).astype(jnp.bfloat16)
    swap = [(i, (i + 1) % cores) for i in range(cores)]

    def expert(gathered):
        rows = gathered[:, :D]
        code = gathered[:, D:D + 3 * EXPERTS]
        weight = jnp.dot(code, select, preferred_element_type=jnp.float32)
        gate_part = jnp.einsum("nd,edf->enf", rows, w_gate, preferred_element_type=jnp.float32)
        up_part = jnp.einsum("nd,edf->enf", rows, w_up, preferred_element_type=jnp.float32)
        hidden = (jax.nn.silu(gate_part) * up_part).astype(jnp.bfloat16)
        result = jnp.einsum("enf,efd->end", hidden, w_down, preferred_element_type=jnp.float32)
        result = result.astype(jnp.bfloat16).astype(jnp.float32)
        return jnp.sum(result * weight.T[:, :, None], axis=0).astype(jnp.bfloat16)

    chunk = positions // CHUNKS
    outs = []
    for c in range(CHUNKS):
        own = lax.all_gather(payload[c * chunk:(c + 1) * chunk], "y", axis=0, tiled=True)
        other = lax.ppermute(own, "core", swap)
        back = expert(other)
        returned = lax.ppermute(back, "core", swap)
        mine = expert(own)
        total = (mine.astype(jnp.float32) + returned.astype(jnp.float32)).astype(jnp.bfloat16)
        outs.append(lax.psum_scatter(total, "y", scatter_dimension=0, tiled=True))
    combined = jnp.concatenate(outs, axis=0)
    return (resid_float + combined.astype(jnp.float32)).astype(jnp.bfloat16)[None]


def solution(mesh):
    devices = mesh.devices
    split = jax.sharding.Mesh(
        devices.reshape(devices.shape[0], devices.shape[1] // 2, 2), ("seq", "y", "core")
    )
    exp = ("y", "core")
    in_specs = (
        P(exp, "seq", None),
        P(exp, "seq", None),
        P(exp, "seq", None),
        P(exp, "seq", None),
        P(),
        P(),
        P(exp, "seq", None),
        P(exp, "seq", None),
        P(exp, None, None),
        P(exp, None, None),
        P(exp, None, None),
    )
    out_specs = P(exp, "seq", None)

    return jax.shard_map(on_device, mesh=split, in_specs=in_specs, out_specs=out_specs, check_vma=False)
```

```python
import jax
import jax.numpy as jnp
from jax import lax
from jax.experimental.layout import Layout, with_layout_constraint
from jax.sharding import PartitionSpec as P


D = 2048
HEADS = 16
HD = 128
EXPERTS = 8
CHUNKS = 2


def block_prefix(state):
    blocks = lax.axis_size("seq")
    pieces = state if blocks == state.shape[0] else state.reshape(blocks, -1)
    gathered = lax.all_to_all(pieces, "seq", split_axis=0, concat_axis=0, tiled=True)
    shifted = jnp.concatenate([jnp.zeros_like(gathered[:1]), gathered[:-1]], axis=0)
    prefixes = lax.cumsum(shifted, axis=0).astype(jnp.bfloat16)
    mine = lax.all_to_all(prefixes, "seq", split_axis=0, concat_axis=0, tiled=True)
    return mine.reshape(state.shape)


def on_device(
    residual_in,
    query_matrix,
    key_vectors,
    value_vectors,
    head_gain,
    norm_gain,
    expert_ids,
    gate_probs,
    w_gate,
    w_up,
    w_down,
):
    positions = residual_in.shape[1]
    queries = query_matrix[0].reshape(positions, HEADS, HD)
    key_rows = key_vectors[0].reshape(positions, HEADS, HD)
    value_rows = value_vectors[0].reshape(positions, HEADS, HD)
    state = jnp.einsum("thd,the->hed", key_rows, value_rows, preferred_element_type=jnp.float32)
    prefix = block_prefix(state)
    causal = jnp.tril(jnp.ones((positions, positions), dtype=bool))
    scores = jnp.einsum("thd,uhd->htu", queries, key_rows, preferred_element_type=jnp.float32)
    weights = jnp.where(causal[None], scores, 0.0).astype(jnp.bfloat16)
    inner = jnp.einsum("htu,uhd->thd", weights, value_rows, preferred_element_type=jnp.float32)
    outer_product = jnp.einsum(
        "thd,hed->the", queries, prefix, preferred_element_type=jnp.float32
    )
    mixed = inner + outer_product
    mean_square = jnp.mean(mixed * mixed, axis=-1, keepdims=True)
    attn = (mixed * lax.rsqrt(mean_square + 1e-06)).reshape(positions, D) * head_gain
    attn = with_layout_constraint(attn, Layout(major_to_minor=(0, 1)))
    resid_float = (
        (residual_in[0].astype(jnp.float32) + attn).astype(jnp.bfloat16).astype(jnp.float32)
    )
    row_square = jnp.mean(resid_float * resid_float, axis=-1, keepdims=True)
    normed = (resid_float * lax.rsqrt(row_square + 1e-06) * norm_gain).astype(jnp.bfloat16)

    route_ids = expert_ids[0]
    route_gates = gate_probs[0]
    experts = jnp.arange(EXPERTS, dtype=jnp.int32)
    table = jnp.sum(
        jnp.where(route_ids[:, :, None] == experts[None, None, :], route_gates[:, :, None], 0.0),
        axis=1,
    )
    me = lax.axis_index("y") * lax.axis_size("core") + lax.axis_index("core")
    local_count = w_gate.shape[0]
    high = table.astype(jnp.bfloat16)
    rest = table - high.astype(jnp.float32)
    middle = rest.astype(jnp.bfloat16)
    low = (rest - middle.astype(jnp.float32)).astype(jnp.bfloat16)
    pad = jnp.zeros((positions, 128 - 3 * EXPERTS), jnp.bfloat16)
    payload = jnp.concatenate([normed, high, middle, low, pad], axis=1)

    columns = jnp.arange(3 * EXPERTS, dtype=jnp.int32) % EXPERTS
    select = (columns[:, None] == me * local_count + jnp.arange(local_count)[None, :]).astype(jnp.bfloat16)
    chips = lax.axis_size("y")
    cores = lax.axis_size("core")
    ring = lax.axis_index("y")
    core = lax.axis_index("core")

    def shift(x, axis, step, size):
        return lax.ppermute(x, axis, [(i, (i + step) % size) for i in range(size)])

    def gather_rows(x):
        n = x.shape[0]
        half = n // 2
        prev = shift(x, "y", 1, chips)
        nxt = shift(x, "y", -1, chips)
        far = jnp.concatenate([shift(prev[:half], "y", 1, chips), shift(nxt[half:], "y", -1, chips)], axis=0)
        relative = jnp.stack([x, nxt, far, prev])
        doubled = jnp.concatenate([relative, relative], axis=0)
        same = lax.dynamic_slice_in_dim(doubled, (chips - ring) % chips, chips, axis=0)
        other = shift(same, "core", 1, cores)
        first = jnp.where(core == 0, same, other)
        second = jnp.where(core == 0, other, same)
        return jnp.stack([first, second], axis=1).reshape(chips * cores * n, x.shape[1])

    chunk = positions // CHUNKS
    outs = []
    for c in range(CHUNKS):
        gathered = gather_rows(payload[c * chunk:(c + 1) * chunk])
        rows = gathered[:, :D]
        code = gathered[:, D:D + 3 * EXPERTS]
        weight = jnp.dot(code, select, preferred_element_type=jnp.float32)
        gate_part = jnp.einsum("nd,edf->enf", rows, w_gate, preferred_element_type=jnp.float32)
        up_part = jnp.einsum("nd,edf->enf", rows, w_up, preferred_element_type=jnp.float32)
        hidden = (jax.nn.silu(gate_part) * up_part).astype(jnp.bfloat16)
        result = jnp.einsum("enf,efd->end", hidden, w_down, preferred_element_type=jnp.float32)
        result = result.astype(jnp.bfloat16).astype(jnp.float32)
        contrib = jnp.sum(result * weight.T[:, :, None], axis=0).astype(jnp.bfloat16)
        outs.append(lax.psum_scatter(contrib, ("y", "core"), scatter_dimension=0, tiled=True))
    combined = jnp.concatenate(outs, axis=0)
    return (resid_float + combined.astype(jnp.float32)).astype(jnp.bfloat16)[None]


def solution(mesh):
    devices = mesh.devices
    split = jax.sharding.Mesh(
        devices.reshape(devices.shape[0], devices.shape[1] // 2, 2), ("seq", "y", "core")
    )
    exp = ("y", "core")
    in_specs = (
        P(exp, "seq", None),
        P(exp, "seq", None),
        P(exp, "seq", None),
        P(exp, "seq", None),
        P(),
        P(),
        P(exp, "seq", None),
        P(exp, "seq", None),
        P(exp, None, None),
        P(exp, None, None),
        P(exp, None, None),
    )
    out_specs = P(exp, "seq", None)

    return jax.shard_map(on_device, mesh=split, in_specs=in_specs, out_specs=out_specs, check_vma=False)
```

```python
import jax
import jax.numpy as jnp
from jax import lax
from jax.experimental.layout import Layout, with_layout_constraint
from jax.sharding import PartitionSpec as P


D = 2048
HEADS = 16
HD = 128
EXPERTS = 8
CHUNKS = 2


def block_prefix(state):
    blocks = lax.axis_size("seq")
    pieces = state if blocks == state.shape[0] else state.reshape(blocks, -1)
    gathered = lax.all_to_all(pieces, "seq", split_axis=0, concat_axis=0, tiled=True)
    shifted = jnp.concatenate([jnp.zeros_like(gathered[:1]), gathered[:-1]], axis=0)
    prefixes = lax.cumsum(shifted, axis=0).astype(jnp.bfloat16)
    mine = lax.all_to_all(prefixes, "seq", split_axis=0, concat_axis=0, tiled=True)
    return mine.reshape(state.shape)


def on_device(
    residual_in,
    query_matrix,
    key_vectors,
    value_vectors,
    head_gain,
    norm_gain,
    expert_ids,
    gate_probs,
    w_gate,
    w_up,
    w_down,
):
    positions = residual_in.shape[1]
    queries = query_matrix[0].reshape(positions, HEADS, HD)
    key_rows = key_vectors[0].reshape(positions, HEADS, HD)
    value_rows = value_vectors[0].reshape(positions, HEADS, HD)
    state = jnp.einsum("thd,the->hed", key_rows, value_rows, preferred_element_type=jnp.float32)
    prefix = block_prefix(state)
    causal = jnp.tril(jnp.ones((positions, positions), dtype=bool))
    scores = jnp.einsum("thd,uhd->htu", queries, key_rows, preferred_element_type=jnp.float32)
    weights = jnp.where(causal[None], scores, 0.0).astype(jnp.bfloat16)
    inner = jnp.einsum("htu,uhd->thd", weights, value_rows, preferred_element_type=jnp.float32)
    outer_product = jnp.einsum(
        "thd,hed->the", queries, prefix, preferred_element_type=jnp.float32
    )
    mixed = inner + outer_product
    mean_square = jnp.mean(mixed * mixed, axis=-1, keepdims=True)
    attn = (mixed * lax.rsqrt(mean_square + 1e-06)).reshape(positions, D) * head_gain
    attn = with_layout_constraint(attn, Layout(major_to_minor=(0, 1)))
    resid_float = (
        (residual_in[0].astype(jnp.float32) + attn).astype(jnp.bfloat16).astype(jnp.float32)
    )
    row_square = jnp.mean(resid_float * resid_float, axis=-1, keepdims=True)
    normed = (resid_float * lax.rsqrt(row_square + 1e-06) * norm_gain).astype(jnp.bfloat16)

    route_ids = expert_ids[0]
    route_gates = gate_probs[0]
    experts = jnp.arange(EXPERTS, dtype=jnp.int32)
    table = jnp.sum(
        jnp.where(route_ids[:, :, None] == experts[None, None, :], route_gates[:, :, None], 0.0),
        axis=1,
    )
    chips = lax.axis_size("y")
    cores = lax.axis_size("core")
    core = lax.axis_index("core")
    me = lax.axis_index("y") * cores + core
    local_count = w_gate.shape[0]
    high = table.astype(jnp.bfloat16)
    rest = table - high.astype(jnp.float32)
    middle = rest.astype(jnp.bfloat16)
    low = (rest - middle.astype(jnp.float32)).astype(jnp.bfloat16)
    pad = jnp.zeros((positions, 128 - 3 * EXPERTS), jnp.bfloat16)
    payload = jnp.concatenate([normed, high, middle, low, pad], axis=1)

    columns = jnp.arange(3 * EXPERTS, dtype=jnp.int32) % EXPERTS
    select = (columns[:, None] == me * local_count + jnp.arange(local_count)[None, :]).astype(jnp.bfloat16)
    chunk = positions // CHUNKS
    outs = []
    for c in range(CHUNKS):
        gathered = lax.all_gather(payload[c * chunk:(c + 1) * chunk], ("y", "core"), axis=0, tiled=True)
        rows = gathered[:, :D]
        code = gathered[:, D:D + 3 * EXPERTS]
        weight = jnp.dot(code, select, preferred_element_type=jnp.float32)
        gate_part = jnp.einsum("nd,edf->enf", rows, w_gate, preferred_element_type=jnp.float32)
        up_part = jnp.einsum("nd,edf->enf", rows, w_up, preferred_element_type=jnp.float32)
        hidden = (jax.nn.silu(gate_part) * up_part).astype(jnp.bfloat16)
        result = jnp.einsum("enf,efd->end", hidden, w_down, preferred_element_type=jnp.float32)
        result = result.astype(jnp.bfloat16).astype(jnp.float32)
        contrib = jnp.sum(result * weight.T[:, :, None], axis=0).astype(jnp.bfloat16)
        paired = contrib.reshape(chips, cores, chunk, D)
        mine = lax.dynamic_index_in_dim(paired, core, axis=1, keepdims=False)
        theirs = lax.dynamic_index_in_dim(paired, (core + 1) % cores, axis=1, keepdims=False)
        received = lax.ppermute(theirs, "core", [(i, (i + 1) % cores) for i in range(cores)])
        total = (mine.astype(jnp.float32) + received.astype(jnp.float32)).astype(jnp.bfloat16)
        combined = lax.psum_scatter(total.reshape(chips * chunk, D), "y", scatter_dimension=0, tiled=True)
        own = resid_float[c * chunk:(c + 1) * chunk]
        outs.append((own + combined.astype(jnp.float32)).astype(jnp.bfloat16))
    return jnp.concatenate(outs, axis=0)[None]


def solution(mesh):
    devices = mesh.devices
    split = jax.sharding.Mesh(
        devices.reshape(devices.shape[0], devices.shape[1] // 2, 2), ("seq", "y", "core")
    )
    exp = ("y", "core")
    in_specs = (
        P(exp, "seq", None),
        P(exp, "seq", None),
        P(exp, "seq", None),
        P(exp, "seq", None),
        P(),
        P(),
        P(exp, "seq", None),
        P(exp, "seq", None),
        P(exp, None, None),
        P(exp, None, None),
        P(exp, None, None),
    )
    out_specs = P(exp, "seq", None)

    return jax.shard_map(on_device, mesh=split, in_specs=in_specs, out_specs=out_specs, check_vma=False)
```

```python
import jax
import jax.numpy as jnp
from jax import lax
from jax.experimental.layout import Layout, with_layout_constraint
from jax.sharding import PartitionSpec as P


D = 2048
HEADS = 16
HD = 128
EXPERTS = 8
CHUNKS = 2


def block_prefix(state):
    blocks = lax.axis_size("seq")
    pieces = state if blocks == state.shape[0] else state.reshape(blocks, -1)
    gathered = lax.all_to_all(pieces, "seq", split_axis=0, concat_axis=0, tiled=True)
    shifted = jnp.concatenate([jnp.zeros_like(gathered[:1]), gathered[:-1]], axis=0)
    prefixes = lax.cumsum(shifted, axis=0).astype(jnp.bfloat16)
    mine = lax.all_to_all(prefixes, "seq", split_axis=0, concat_axis=0, tiled=True)
    return mine.reshape(state.shape)


def on_device(
    residual_in,
    query_matrix,
    key_vectors,
    value_vectors,
    head_gain,
    norm_gain,
    expert_ids,
    gate_probs,
    w_gate,
    w_up,
    w_down,
):
    positions = residual_in.shape[1]
    queries = query_matrix[0].reshape(positions, HEADS, HD)
    key_rows = key_vectors[0].reshape(positions, HEADS, HD)
    value_rows = value_vectors[0].reshape(positions, HEADS, HD)
    state = jnp.einsum("thd,the->hed", key_rows, value_rows, preferred_element_type=jnp.float32)
    prefix = block_prefix(state)
    causal = jnp.tril(jnp.ones((positions, positions), dtype=bool))
    scores = jnp.einsum("thd,uhd->htu", queries, key_rows, preferred_element_type=jnp.float32)
    weights = jnp.where(causal[None], scores, 0.0).astype(jnp.bfloat16)
    inner = jnp.einsum("htu,uhd->thd", weights, value_rows, preferred_element_type=jnp.float32)
    outer_product = jnp.einsum(
        "thd,hed->the", queries, prefix, preferred_element_type=jnp.float32
    )
    mixed = inner + outer_product
    mean_square = jnp.mean(mixed * mixed, axis=-1, keepdims=True)
    attn = (mixed * lax.rsqrt(mean_square + 1e-06)).reshape(positions, D) * head_gain
    attn = with_layout_constraint(attn, Layout(major_to_minor=(0, 1)))
    resid_float = (
        (residual_in[0].astype(jnp.float32) + attn).astype(jnp.bfloat16).astype(jnp.float32)
    )
    row_square = jnp.mean(resid_float * resid_float, axis=-1, keepdims=True)
    normed = (resid_float * lax.rsqrt(row_square + 1e-06) * norm_gain).astype(jnp.bfloat16)

    route_ids = expert_ids[0]
    route_gates = gate_probs[0]
    experts = jnp.arange(EXPERTS, dtype=jnp.int32)
    table = jnp.sum(
        jnp.where(route_ids[:, :, None] == experts[None, None, :], route_gates[:, :, None], 0.0),
        axis=1,
    )
    chips = lax.axis_size("y")
    cores = lax.axis_size("core")
    core = lax.axis_index("core")
    me = lax.axis_index("y") * cores + core
    local_count = w_gate.shape[0]
    high = table.astype(jnp.bfloat16)
    rest = table - high.astype(jnp.float32)
    middle = rest.astype(jnp.bfloat16)
    low = (rest - middle.astype(jnp.float32)).astype(jnp.bfloat16)
    pad = jnp.zeros((positions, 128 - 3 * EXPERTS), jnp.bfloat16)
    payload = jnp.concatenate([normed, high, middle, low, pad], axis=1)

    columns = jnp.arange(3 * EXPERTS, dtype=jnp.int32) % EXPERTS
    select = (columns[:, None] == me * local_count + jnp.arange(local_count)[None, :]).astype(jnp.bfloat16)
    chunk = positions // CHUNKS
    outs = []
    pending = None

    def scatter(c, total):
        combined = lax.psum_scatter(total.reshape(chips * chunk, D), "y", scatter_dimension=0, tiled=True)
        own = resid_float[c * chunk:(c + 1) * chunk]
        outs.append((own + combined.astype(jnp.float32)).astype(jnp.bfloat16))

    for c in range(CHUNKS):
        gathered = lax.all_gather(payload[c * chunk:(c + 1) * chunk], ("y", "core"), axis=0, tiled=True)
        if pending is not None:
            gathered, pending = lax.optimization_barrier((gathered, pending))
            scatter(c - 1, pending)
        rows = gathered[:, :D]
        code = gathered[:, D:D + 3 * EXPERTS]
        weight = jnp.dot(code, select, preferred_element_type=jnp.float32)
        gate_part = jnp.einsum("nd,edf->enf", rows, w_gate, preferred_element_type=jnp.float32)
        up_part = jnp.einsum("nd,edf->enf", rows, w_up, preferred_element_type=jnp.float32)
        hidden = (jax.nn.silu(gate_part) * up_part).astype(jnp.bfloat16)
        result = jnp.einsum("enf,efd->end", hidden, w_down, preferred_element_type=jnp.float32)
        result = result.astype(jnp.bfloat16).astype(jnp.float32)
        contrib = jnp.sum(result * weight.T[:, :, None], axis=0).astype(jnp.bfloat16)
        paired = contrib.reshape(chips, cores, chunk, D)
        mine = lax.dynamic_index_in_dim(paired, core, axis=1, keepdims=False)
        theirs = lax.dynamic_index_in_dim(paired, (core + 1) % cores, axis=1, keepdims=False)
        received = lax.ppermute(theirs, "core", [(i, (i + 1) % cores) for i in range(cores)])
        pending = (mine.astype(jnp.float32) + received.astype(jnp.float32)).astype(jnp.bfloat16)
    scatter(CHUNKS - 1, pending)
    return jnp.concatenate(outs, axis=0)[None]


def solution(mesh):
    devices = mesh.devices
    split = jax.sharding.Mesh(
        devices.reshape(devices.shape[0], devices.shape[1] // 2, 2), ("seq", "y", "core")
    )
    exp = ("y", "core")
    in_specs = (
        P(exp, "seq", None),
        P(exp, "seq", None),
        P(exp, "seq", None),
        P(exp, "seq", None),
        P(),
        P(),
        P(exp, "seq", None),
        P(exp, "seq", None),
        P(exp, None, None),
        P(exp, None, None),
        P(exp, None, None),
    )
    out_specs = P(exp, "seq", None)

    return jax.shard_map(on_device, mesh=split, in_specs=in_specs, out_specs=out_specs, check_vma=False)
```

```python
import jax
import jax.numpy as jnp
from jax import lax
from jax.experimental.layout import Layout, with_layout_constraint
from jax.sharding import PartitionSpec as P


D = 2048
HEADS = 16
HD = 128
EXPERTS = 8
CHUNKS = 2


def block_prefix(state):
    blocks = lax.axis_size("seq")
    pieces = state if blocks == state.shape[0] else state.reshape(blocks, -1)
    gathered = lax.all_to_all(pieces, "seq", split_axis=0, concat_axis=0, tiled=True)
    shifted = jnp.concatenate([jnp.zeros_like(gathered[:1]), gathered[:-1]], axis=0)
    prefixes = lax.cumsum(shifted, axis=0).astype(jnp.bfloat16)
    mine = lax.all_to_all(prefixes, "seq", split_axis=0, concat_axis=0, tiled=True)
    return mine.reshape(state.shape)


def on_device(
    residual_in,
    query_matrix,
    key_vectors,
    value_vectors,
    head_gain,
    norm_gain,
    expert_ids,
    gate_probs,
    w_gate,
    w_up,
    w_down,
):
    positions = residual_in.shape[1]
    queries = query_matrix[0].reshape(positions, HEADS, HD)
    key_rows = key_vectors[0].reshape(positions, HEADS, HD)
    value_rows = value_vectors[0].reshape(positions, HEADS, HD)
    state = jnp.einsum("thd,the->hed", key_rows, value_rows, preferred_element_type=jnp.float32)
    prefix = block_prefix(state)
    causal = jnp.tril(jnp.ones((positions, positions), dtype=bool))
    scores = jnp.einsum("thd,uhd->htu", queries, key_rows, preferred_element_type=jnp.float32)
    weights = jnp.where(causal[None], scores, 0.0).astype(jnp.bfloat16)
    inner = jnp.einsum("htu,uhd->thd", weights, value_rows, preferred_element_type=jnp.float32)
    outer_product = jnp.einsum(
        "thd,hed->the", queries, prefix, preferred_element_type=jnp.float32
    )
    mixed = inner + outer_product
    mean_square = jnp.mean(mixed * mixed, axis=-1, keepdims=True)
    attn = (mixed * lax.rsqrt(mean_square + 1e-06)).reshape(positions, D) * head_gain
    attn = with_layout_constraint(attn, Layout(major_to_minor=(0, 1)))
    resid_float = (
        (residual_in[0].astype(jnp.float32) + attn).astype(jnp.bfloat16).astype(jnp.float32)
    )
    row_square = jnp.mean(resid_float * resid_float, axis=-1, keepdims=True)
    normed = (resid_float * lax.rsqrt(row_square + 1e-06) * norm_gain).astype(jnp.bfloat16)

    route_ids = expert_ids[0]
    route_gates = gate_probs[0]
    experts = jnp.arange(EXPERTS, dtype=jnp.int32)
    table = jnp.sum(
        jnp.where(route_ids[:, :, None] == experts[None, None, :], route_gates[:, :, None], 0.0),
        axis=1,
    )
    groups = lax.axis_size("exp")
    me = lax.axis_index("exp")
    local_count = w_gate.shape[0]
    high = table.astype(jnp.bfloat16)
    rest = table - high.astype(jnp.float32)
    middle = rest.astype(jnp.bfloat16)
    low = (rest - middle.astype(jnp.float32)).astype(jnp.bfloat16)
    codes = jnp.concatenate([high, middle, low], axis=1)
    width = 3 * EXPERTS * CHUNKS
    packed = codes.reshape(positions // CHUNKS, width)
    pad = jnp.zeros((positions // CHUNKS, 128 - width), jnp.bfloat16)

    columns = jnp.arange(3 * EXPERTS, dtype=jnp.int32) % EXPERTS
    select = (columns[:, None] == me * local_count + jnp.arange(local_count)[None, :]).astype(jnp.bfloat16)
    chunk = positions // CHUNKS
    outs = []
    for c in range(CHUNKS):
        part = normed[c * chunk:(c + 1) * chunk]
        if c == 0:
            part = jnp.concatenate([part, packed, pad], axis=1)
        gathered = lax.all_gather(part, "exp", axis=0, tiled=True)
        if c == 0:
            all_codes = gathered[:, D:D + width].reshape(groups, positions, 3 * EXPERTS)
        rows = gathered[:, :D]
        code = all_codes[:, c * chunk:(c + 1) * chunk].reshape(groups * chunk, 3 * EXPERTS)
        weight = jnp.dot(code, select, preferred_element_type=jnp.float32)
        gate_part = jnp.einsum("nd,edf->enf", rows, w_gate, preferred_element_type=jnp.float32)
        up_part = jnp.einsum("nd,edf->enf", rows, w_up, preferred_element_type=jnp.float32)
        hidden = (jax.nn.silu(gate_part) * up_part).astype(jnp.bfloat16)
        result = jnp.einsum("enf,efd->end", hidden, w_down, preferred_element_type=jnp.float32)
        result = result.astype(jnp.bfloat16).astype(jnp.float32)
        contrib = jnp.sum(result * weight.T[:, :, None], axis=0).astype(jnp.bfloat16)
        combined = lax.psum_scatter(contrib, "exp", scatter_dimension=0, tiled=True)
        own = resid_float[c * chunk:(c + 1) * chunk]
        outs.append((own + combined.astype(jnp.float32)).astype(jnp.bfloat16))
    return jnp.concatenate(outs, axis=0)[None]


def solution(mesh):
    in_specs = (
        P("exp", "seq", None),
        P("exp", "seq", None),
        P("exp", "seq", None),
        P("exp", "seq", None),
        P(),
        P(),
        P("exp", "seq", None),
        P("exp", "seq", None),
        P("exp", None, None),
        P("exp", None, None),
        P("exp", None, None),
    )
    out_specs = P("exp", "seq", None)

    return jax.shard_map(on_device, mesh=mesh, in_specs=in_specs, out_specs=out_specs, check_vma=False)
```

```python
import jax
import jax.numpy as jnp
from jax import lax
from jax.experimental.layout import Layout, with_layout_constraint
from jax.sharding import PartitionSpec as P


D = 2048
HEADS = 16
HD = 128
EXPERTS = 8
CHUNKS = 2


def block_prefix(state):
    blocks = lax.axis_size("seq")
    pieces = state if blocks == state.shape[0] else state.reshape(blocks, -1)
    gathered = lax.all_to_all(pieces, "seq", split_axis=0, concat_axis=0, tiled=True)
    shifted = jnp.concatenate([jnp.zeros_like(gathered[:1]), gathered[:-1]], axis=0)
    prefixes = lax.cumsum(shifted, axis=0).astype(jnp.bfloat16)
    mine = lax.all_to_all(prefixes, "seq", split_axis=0, concat_axis=0, tiled=True)
    return mine.reshape(state.shape)


def on_device(
    residual_in,
    query_matrix,
    key_vectors,
    value_vectors,
    head_gain,
    norm_gain,
    expert_ids,
    gate_probs,
    w_gate,
    w_up,
    w_down,
):
    positions = residual_in.shape[1]
    queries = query_matrix[0].reshape(positions, HEADS, HD)
    key_rows = key_vectors[0].reshape(positions, HEADS, HD)
    value_rows = value_vectors[0].reshape(positions, HEADS, HD)
    state = jnp.einsum("thd,the->hed", key_rows, value_rows, preferred_element_type=jnp.float32)
    prefix = block_prefix(state)
    causal = jnp.tril(jnp.ones((positions, positions), dtype=bool))
    scores = jnp.einsum("thd,uhd->htu", queries, key_rows, preferred_element_type=jnp.float32)
    weights = jnp.where(causal[None], scores, 0.0).astype(jnp.bfloat16)
    inner = jnp.einsum("htu,uhd->thd", weights, value_rows, preferred_element_type=jnp.float32)
    def finish(t0, t1, after=None):
        q, own_inner, state_prefix, own_resid = queries[t0:t1], inner[t0:t1], prefix, residual_in[0, t0:t1]
        if after is not None:
            after, q, own_inner, state_prefix, own_resid = lax.optimization_barrier(
                (after, q, own_inner, state_prefix, own_resid))
        outer_product = jnp.einsum(
            "thd,hed->the", q, state_prefix, preferred_element_type=jnp.float32
        )
        mixed = own_inner + outer_product
        mean_square = jnp.mean(mixed * mixed, axis=-1, keepdims=True)
        attn = (mixed * lax.rsqrt(mean_square + 1e-06)).reshape(t1 - t0, D) * head_gain
        attn = with_layout_constraint(attn, Layout(major_to_minor=(0, 1)))
        resid = (
            (own_resid.astype(jnp.float32) + attn).astype(jnp.bfloat16).astype(jnp.float32)
        )
        row_square = jnp.mean(resid * resid, axis=-1, keepdims=True)
        normed = (resid * lax.rsqrt(row_square + 1e-06) * norm_gain).astype(jnp.bfloat16)
        return resid, normed, after

    route_ids = expert_ids[0]
    route_gates = gate_probs[0]
    experts = jnp.arange(EXPERTS, dtype=jnp.int32)
    table = jnp.sum(
        jnp.where(route_ids[:, :, None] == experts[None, None, :], route_gates[:, :, None], 0.0),
        axis=1,
    )
    groups = lax.axis_size("exp")
    me = lax.axis_index("exp")
    local_count = w_gate.shape[0]
    high = table.astype(jnp.bfloat16)
    rest = table - high.astype(jnp.float32)
    middle = rest.astype(jnp.bfloat16)
    low = (rest - middle.astype(jnp.float32)).astype(jnp.bfloat16)
    codes = jnp.concatenate([high, middle, low], axis=1)
    width = 3 * EXPERTS * CHUNKS
    packed = codes.reshape(positions // CHUNKS, width)
    pad = jnp.zeros((positions // CHUNKS, 128 - width), jnp.bfloat16)

    columns = jnp.arange(3 * EXPERTS, dtype=jnp.int32) % EXPERTS
    select = (columns[:, None] == me * local_count + jnp.arange(local_count)[None, :]).astype(jnp.bfloat16)
    chunk = positions // CHUNKS
    finished = []
    parts = []
    for c in range(CHUNKS):
        resid, normed, held = finish(c * chunk, (c + 1) * chunk, parts[-1] if parts else None)
        if held is not None:
            parts[-1] = held
        part = normed if c else jnp.concatenate([normed, packed, pad], axis=1)
        finished.append(resid)
        parts.append(part)
    outs = []
    for c in range(CHUNKS):
        part = parts[c]
        gathered = lax.all_gather(part, "exp", axis=0, tiled=True)
        if c == 0:
            all_codes = gathered[:, D:D + width].reshape(groups, positions, 3 * EXPERTS)
        rows = gathered[:, :D]
        code = all_codes[:, c * chunk:(c + 1) * chunk].reshape(groups * chunk, 3 * EXPERTS)
        weight = jnp.dot(code, select, preferred_element_type=jnp.float32)
        gate_part = jnp.einsum("nd,edf->enf", rows, w_gate, preferred_element_type=jnp.float32)
        up_part = jnp.einsum("nd,edf->enf", rows, w_up, preferred_element_type=jnp.float32)
        hidden = (jax.nn.silu(gate_part) * up_part).astype(jnp.bfloat16)
        result = jnp.einsum("enf,efd->end", hidden, w_down, preferred_element_type=jnp.float32)
        result = result.astype(jnp.bfloat16).astype(jnp.float32)
        contrib = jnp.sum(result * weight.T[:, :, None], axis=0).astype(jnp.bfloat16)
        combined = lax.psum_scatter(contrib, "exp", scatter_dimension=0, tiled=True)
        own = finished[c]
        outs.append((own + combined.astype(jnp.float32)).astype(jnp.bfloat16))
    return jnp.concatenate(outs, axis=0)[None]


def solution(mesh):
    in_specs = (
        P("exp", "seq", None),
        P("exp", "seq", None),
        P("exp", "seq", None),
        P("exp", "seq", None),
        P(),
        P(),
        P("exp", "seq", None),
        P("exp", "seq", None),
        P("exp", None, None),
        P("exp", None, None),
        P("exp", None, None),
    )
    out_specs = P("exp", "seq", None)

    return jax.shard_map(on_device, mesh=mesh, in_specs=in_specs, out_specs=out_specs, check_vma=False)
```
